32 devices in a mesh: win: 4 (over y, x), chan: 8 (over z, core).
Axes of the slice: x: 2, y: 2, z: 4, core: 2. Of those that a mesh axis runs over, the one named last changes fastest.
Arguments:
- source_traces: bfloat16 [4, 1024, 1536], P('win', 'chan'), may hold values from -60 to 60, as said below
- receiver_traces: bfloat16 [4, 8, 1536], P('win', 'chan'), may hold values from -60 to 60, as said below
- owners: int32 [4], replicated, may hold values from 0 to 7
- source_alive: int32 [1024], P('chan'), may hold values 0 or 1
- receiver_alive: int32 [8], P('chan'), may hold values 0 or 1
Outputs:
- gathers: float32 [4, 128, 8, 1501], P(None, 'win', 'chan')
The draws below stay inside these ranges and needn't reach their ends.
Inputs may be any that keep to these rules, and one draw needn't show every extreme that they name: `source_traces`: trace samples. `receiver_traces`: trace samples.
All inputs are finite; a program needn't handle non-finite values. No bound on the sum of `source_alive` or of `receiver_alive` on one device may be relied on, other than what follows from the above.
Results may differ from the reference program's by a relative error of at most 0.0041.
Values may be sent and summed in bfloat16 or wider, within the bound.
No kernel may reach another device: no remote copies, remote signals or barrier semaphores. Data moves between devices by JAX's collectives and lax.ppermute only.
A program may use at most 64 MiB of HBM per device.

```python
import math
import jax
import jax.numpy as jnp
from jax import lax

SRC = 128
NT = 1536
HALF = 750
STEPS = 4
WINDOWS = 4
VIRTUAL_EMITTERS = 1024
RECEIVER_LINES = 8
N_CHAN = 8


def transient_recordings(key, row_entries):
    first_key, second_key = jax.random.split(jax.random.fold_in(key, 17))
    runs = NT // 64
    base = jnp.clip(jax.random.normal(first_key, (WINDOWS, row_entries, runs, 64), jnp.float32), -6.0, 6.0)
    levels = jnp.exp(jax.random.uniform(second_key, (WINDOWS, row_entries, runs, 1), jnp.float32, math.log(0.1), math.log(10.0)))
    return (base * levels).reshape(WINDOWS, row_entries, NT).astype(jnp.bfloat16)


def draw_source_traces(key, part):
    return transient_recordings(jax.random.fold_in(key, 1), VIRTUAL_EMITTERS)


def draw_receiver_traces(key, part):
    return transient_recordings(jax.random.fold_in(key, 2), RECEIVER_LINES)


def set_ends(array, stream_key, smallest, top_value):
    longest = array.shape.index(max(array.shape))
    spots = []
    for shift in (0, 1):
        where = [jax.random.randint(jax.random.fold_in(stream_key, axis), (), 0, length) for axis, length in enumerate(array.shape)]
        where[longest] = (where[longest] + shift) % array.shape[longest]
        spots.append(tuple(where))
    return array.at[spots[0]].set(smallest).at[spots[1]].set(top_value)


def setup_inputs(seed: int = 0) -> dict:
    key_list = jax.random.split(jax.random.key(seed), 6)
    source_traces = draw_source_traces(jax.random.fold_in(key_list[5], 71), 0)
    receiver_traces = draw_receiver_traces(jax.random.fold_in(key_list[5], 71), 0)
    owners = set_ends(jax.random.randint(key_list[2], (STEPS,), 0, N_CHAN), jax.random.fold_in(key_list[2], 1), 0, N_CHAN - 1).astype(jnp.int32)
    source_alive = set_ends((jax.random.randint(key_list[3], (VIRTUAL_EMITTERS,), 0, 10) < 9).astype(jnp.int32), jax.random.fold_in(key_list[3], 1), 0, 1)
    receiver_alive = set_ends((jax.random.randint(key_list[4], (RECEIVER_LINES,), 0, 10) < 9).astype(jnp.int32), jax.random.fold_in(key_list[4], 1), 0, 1)
    return dict(source_traces=source_traces, receiver_traces=receiver_traces, owners=owners, source_alive=source_alive, receiver_alive=receiver_alive)


epsilon_energy = 1e-06
band_limit = 256

def spectral_flatten(traces):
    row_entries, length = traces.shape
    values = traces.astype(jnp.float32).reshape(row_entries, length // 64, 64)
    power = lax.optimization_barrier(jnp.mean(values * values, axis=-1, keepdims=True))
    return (values * lax.rsqrt(power + epsilon_energy)).reshape(row_entries, length)

def pad_receivers(white, half, lag_count):
    width = min(band_limit, lag_count)
    blocks = -(-lag_count // width)
    return jnp.pad(white, ((0, 0), (half, half + blocks * width - lag_count + 1)))

def lag_bands(padded, start, width, length):
    count = padded.shape[0]
    piece = lax.dynamic_slice_in_dim(padded, start, length + width, 1)
    tiled = jnp.tile(piece, (1, width + 1))
    flat = tiled[:, :width * (length + width + 1)]
    return flat.reshape(count, width, length + width + 1)[:, :, :length]

def correlate(sources, padded, lag_count):
    length = sources.shape[1]
    count = padded.shape[0]
    width = min(band_limit, lag_count)
    blocks = -(-lag_count // width)
    starts = jnp.arange(blocks, dtype=jnp.int32) * width

    def one_band(start):
        band = lag_bands(padded, start, width, length)
        return jnp.einsum('st,rjt->srj', sources.astype(jnp.float32), band.astype(jnp.float32))
    pieces = lax.map(one_band, starts)
    joined = jnp.moveaxis(pieces, 0, 2).reshape(sources.shape[0], count, blocks * width)
    return joined[:, :, :lag_count]

def reference(source_traces, receiver_traces, owners, source_alive, receiver_alive):
    lag_count = 2 * HALF + 1
    live_rcv = receiver_alive.astype(jnp.float32)[:, None]
    live_src = source_alive.astype(jnp.float32)
    scale = 1.0 / math.sqrt(WINDOWS * NT)
    results = []
    for step in range(STEPS):
        first = (owners[step] * SRC).astype(jnp.int32)
        alive = lax.dynamic_slice_in_dim(live_src, first, SRC, 0)[:, None]

        def window(pair):
            src_rows, rcv_rows = pair
            block = lax.dynamic_slice_in_dim(src_rows, first, SRC, 0)
            white_src = (spectral_flatten(block) * alive).astype(jnp.bfloat16)
            whitened_receiver = (spectral_flatten(rcv_rows) * live_rcv).astype(jnp.bfloat16)
            padded = pad_receivers(whitened_receiver, HALF, lag_count)
            return correlate(white_src, padded, lag_count)
        parts = lax.map(window, (source_traces, receiver_traces))
        results.append(lax.optimization_barrier(jnp.sum(parts, axis=0)))
    return jnp.stack(results) * scale
```

```python
import functools
import math

import jax
import jax.numpy as jnp
from jax import lax
from jax.experimental import pallas as pl
from jax.experimental.pallas import tpu as pltpu
from jax.sharding import PartitionSpec as P

HALF = 750
STEPS = 4
CHUNK = 256

epsilon_energy = 1e-06


def spectral_flatten(traces):
    row_entries, length = traces.shape
    values = traces.astype(jnp.float32).reshape(row_entries, length // 64, 64)
    power = jnp.mean(values * values, axis=-1, keepdims=True)
    return (values * lax.rsqrt(power + epsilon_energy)).reshape(row_entries, length)


def corr_kernel(x_ref, p_ref, o_ref, *, nt, cols, lags, scale):
    n_win, m, _ = x_ref.shape
    width = CHUNK + cols
    acc = jnp.zeros((m, cols), jnp.float32)
    for w in range(n_win):
        for i in range(nt // CHUNK):
            t0 = i * CHUNK
            start = nt - CHUNK - t0
            v = p_ref[w, :, start:start + width]
            rows = jnp.broadcast_to(v, (CHUNK, width))
            rolled = pltpu.roll(rows, 0, 1, stride=1, stride_axis=0)
            band = rolled[:, CHUNK:CHUNK + cols].astype(jnp.bfloat16)
            acc = acc + jnp.dot(
                x_ref[w, :, t0:t0 + CHUNK], band, preferred_element_type=jnp.float32
            )
    o_ref[...] = (acc * scale)[:, :lags]


def correlate(x, p, lags, scale):
    n_win, m, nt = x.shape
    cols = p.shape[-1] - nt
    kern = functools.partial(corr_kernel, nt=nt, cols=cols, lags=lags, scale=scale)
    return pl.pallas_call(
        kern,
        out_shape=jax.ShapeDtypeStruct((m, lags), jnp.float32),
        compiler_params=pltpu.CompilerParams(vmem_limit_bytes=48 * 1024 * 1024),
    )(x, p)


def body(source_traces, receiver_traces, owners, source_alive, receiver_alive):
    lag_count = 2 * HALF + 1
    n_win = lax.axis_size("win")
    nt = source_traces.shape[2]
    rows = source_traces.shape[1] // n_win
    cols = -(-lag_count // 128) * 128
    scale = 1.0 / math.sqrt(n_win * nt)

    own_white = (
        spectral_flatten(source_traces[0]) * source_alive.astype(jnp.float32)[:, None]
    ).astype(jnp.bfloat16)
    own_white = own_white[:, ::-1].reshape(n_win, rows, nt)
    mine = lax.all_to_all(own_white, "win", 0, 0, tiled=True)
    me = lax.axis_index("chan")
    pick = (owners == me).astype(jnp.bfloat16)
    contrib = mine[:, None] * pick[None, :, None, None]
    blocks = lax.psum(contrib, "chan")
    x = blocks.reshape(n_win, STEPS * rows, nt)

    rcv_white = (
        spectral_flatten(receiver_traces[0]) * receiver_alive.astype(jnp.float32)[:, None]
    ).astype(jnp.bfloat16)
    rcv_all = lax.all_gather(rcv_white, "win", axis=0, tiled=True)
    padded = jnp.pad(
        rcv_all.astype(jnp.float32), ((0, 0), (HALF + 1, cols - HALF - 1))
    )[:, None, :]

    out = correlate(x, padded, lag_count, scale)
    return out.reshape(STEPS, rows, 1, lag_count)


def solution(mesh):
    placed = (P("win", "chan", None), P("win", "chan", None), P(), P("chan"), P("chan"))
    return jax.shard_map(
        body, mesh=mesh, in_specs=placed, out_specs=P(None, "win", "chan", None), check_vma=False
    )
```

```python
import functools
import math

import jax
import jax.numpy as jnp
from jax import lax
from jax.experimental import pallas as pl
from jax.experimental.pallas import tpu as pltpu
from jax.sharding import Mesh, PartitionSpec as P

HALF = 750
STEPS = 4
CHUNK = 256

epsilon_energy = 1e-06


def spectral_flatten(traces):
    row_entries, length = traces.shape
    values = traces.astype(jnp.float32).reshape(row_entries, length // 64, 64)
    power = jnp.mean(values * values, axis=-1, keepdims=True)
    return (values * lax.rsqrt(power + epsilon_energy)).reshape(row_entries, length)


def corr_kernel(x_ref, p_ref, o_ref, *, nt, cols, lags, scale):
    n_win, m, _ = x_ref.shape
    width = CHUNK + cols
    acc = jnp.zeros((m, cols), jnp.float32)
    for w in range(n_win):
        for i in range(nt // CHUNK):
            t0 = i * CHUNK
            start = nt - CHUNK - t0
            v = p_ref[w, :, start:start + width]
            rows = jnp.broadcast_to(v, (CHUNK, width))
            rolled = pltpu.roll(rows, 0, 1, stride=1, stride_axis=0)
            band = rolled[:, CHUNK:CHUNK + cols].astype(jnp.bfloat16)
            acc = acc + jnp.dot(
                x_ref[w, :, t0:t0 + CHUNK], band, preferred_element_type=jnp.float32
            )
    o_ref[...] = (acc * scale)[:, :lags]


def correlate(x, p, lags, scale):
    n_win, m, nt = x.shape
    cols = p.shape[-1] - nt
    kern = functools.partial(corr_kernel, nt=nt, cols=cols, lags=lags, scale=scale)
    return pl.pallas_call(
        kern,
        out_shape=jax.ShapeDtypeStruct((m, lags), jnp.float32),
        compiler_params=pltpu.CompilerParams(vmem_limit_bytes=48 * 1024 * 1024),
    )(x, p)


def body(source_traces, receiver_traces, owners, source_alive, receiver_alive):
    lag_count = 2 * HALF + 1
    n_win = lax.axis_size("win")
    n_core = lax.axis_size("core")
    nt = source_traces.shape[2]
    rows = source_traces.shape[1] // n_win
    half = rows // n_core
    cols = -(-lag_count // 128) * 128
    per = -(-nt // half)
    extra = -(-per // 128) * 128
    scale = 1.0 / math.sqrt(n_win * nt)

    own_white = (
        spectral_flatten(source_traces[0]) * source_alive.astype(jnp.float32)[:, None]
    ).astype(jnp.bfloat16)
    own_white = own_white[:, ::-1].reshape(n_win * n_core, half, nt)
    rcv_white = (
        spectral_flatten(receiver_traces[0]) * receiver_alive.astype(jnp.float32)[:, None]
    ).astype(jnp.bfloat16)
    rcv_rows = jnp.pad(rcv_white.reshape(-1), (0, half * per - nt)).reshape(half, per)
    rcv_rows = jnp.pad(rcv_rows, ((0, 0), (0, extra - per)))
    payload = jnp.concatenate(
        [own_white, jnp.broadcast_to(rcv_rows, (n_win * n_core, half, extra))], axis=2
    )
    got = lax.all_to_all(payload, ("win", "core"), 0, 0, tiled=True)
    got = got.reshape(n_win, n_core, half, nt + extra)

    my_core = lax.axis_index("core")
    my_chip = lax.axis_index("zz")
    chans = my_chip * n_core + jnp.arange(n_core, dtype=owners.dtype)
    pick = (owners[:, None] == chans[None, :]).astype(jnp.bfloat16)
    src = got[..., :nt]
    contrib = jnp.einsum("wqst,kq->wkst", src, pick, preferred_element_type=jnp.bfloat16)
    blocks = lax.psum(contrib, "zz")
    blocks = lax.all_gather(blocks, "core", axis=2, tiled=True)
    x = blocks.reshape(n_win, STEPS * rows, nt)

    mine = lax.dynamic_index_in_dim(got, my_core, axis=1, keepdims=False)
    rcv_all = mine[:, :, nt:nt + per].reshape(n_win, half * per)[:, :nt]
    padded = jnp.pad(
        rcv_all.astype(jnp.float32), ((0, 0), (HALF + 1, cols - HALF - 1))
    )[:, None, :]

    out = correlate(x, padded, lag_count, scale)
    return out.reshape(STEPS, rows, 1, lag_count)


def solution(mesh):
    n_chan = mesh.shape["chan"]
    devices = mesh.devices.reshape(mesh.shape["win"], n_chan // 2, 2)
    sub = Mesh(devices, ("win", "zz", "core"))
    chan = ("zz", "core")
    placed = (P("win", chan, None), P("win", chan, None), P(), P(chan), P(chan))
    return jax.shard_map(
        body, mesh=sub, in_specs=placed, out_specs=P(None, "win", chan, None), check_vma=False
    )
```

```python
import functools
import math

import jax
import jax.numpy as jnp
from jax import lax
from jax.experimental import pallas as pl
from jax.experimental.pallas import tpu as pltpu
from jax.sharding import Mesh, PartitionSpec as P

HALF = 750
STEPS = 4
CHUNK = 256

epsilon_energy = 1e-06


def spectral_flatten(traces):
    row_entries, length = traces.shape
    values = traces.astype(jnp.float32).reshape(row_entries, length // 64, 64)
    power = jnp.mean(values * values, axis=-1, keepdims=True)
    return (values * lax.rsqrt(power + epsilon_energy)).reshape(row_entries, length)


def corr_kernel(x_ref, p_ref, o_ref, *, nt, cols, lags, scale):
    n_win, m, _ = x_ref.shape
    width = CHUNK + cols
    acc = jnp.zeros((m, cols), jnp.float32)
    for w in range(n_win):
        for i in range(nt // CHUNK):
            t0 = i * CHUNK
            start = nt - CHUNK - t0
            v = p_ref[w, :, start:start + width]
            rows = jnp.broadcast_to(v, (CHUNK, width))
            rolled = pltpu.roll(rows, 0, 1, stride=1, stride_axis=0)
            band = rolled[:, CHUNK:CHUNK + cols].astype(jnp.bfloat16)
            acc = acc + jnp.dot(
                x_ref[w, :, t0:t0 + CHUNK], band, preferred_element_type=jnp.float32
            )
    o_ref[...] = (acc * scale)[:, :lags]


def correlate(x, p, lags, scale):
    n_win, m, nt = x.shape
    cols = p.shape[-1] - nt
    kern = functools.partial(corr_kernel, nt=nt, cols=cols, lags=lags, scale=scale)
    return pl.pallas_call(
        kern,
        out_shape=jax.ShapeDtypeStruct((m, lags), jnp.float32),
        compiler_params=pltpu.CompilerParams(vmem_limit_bytes=48 * 1024 * 1024),
    )(x, p)


def body(source_traces, receiver_traces, owners, source_alive, receiver_alive):
    lag_count = 2 * HALF + 1
    n_win = lax.axis_size("win")
    n_core = lax.axis_size("core")
    nt = source_traces.shape[2]
    rows = source_traces.shape[1] // n_win
    half = rows // n_core
    cols = -(-lag_count // 128) * 128
    per = -(-nt // half)
    extra = -(-per // 128) * 128
    scale = 1.0 / math.sqrt(n_win * nt)

    own_white = (
        spectral_flatten(source_traces[0]) * source_alive.astype(jnp.float32)[:, None]
    ).astype(jnp.bfloat16)
    own_white = own_white[:, ::-1].reshape(n_win * n_core, half, nt)
    rcv_white = (
        spectral_flatten(receiver_traces[0]) * receiver_alive.astype(jnp.float32)[:, None]
    ).astype(jnp.bfloat16)
    rcv_rows = jnp.pad(rcv_white.reshape(-1), (0, half * per - nt)).reshape(half, per)
    rcv_rows = jnp.pad(rcv_rows, ((0, 0), (0, extra - per)))
    payload = jnp.concatenate(
        [own_white, jnp.broadcast_to(rcv_rows, (n_win * n_core, half, extra))], axis=2
    )
    got = lax.all_to_all(payload, ("win", "core"), 0, 0, tiled=True)
    got = got.reshape(n_win, n_core, half, nt + extra)

    my_core = lax.axis_index("core")
    my_chip = lax.axis_index("zz")
    n_chip = lax.axis_size("zz")
    src = got[..., :nt]
    ring = [src] + [
        lax.ppermute(src, "zz", [(i, (i + j) % n_chip) for i in range(n_chip)])
        for j in range(1, n_chip)
    ]
    ring = jnp.stack(ring)
    picked = []
    for k in range(STEPS):
        chip = owners[k] // n_core
        core = owners[k] % n_core
        at = lax.rem(my_chip - chip + n_chip, n_chip)
        block = lax.dynamic_index_in_dim(ring, at, 0, keepdims=False)
        picked.append(lax.dynamic_index_in_dim(block, core, 1, keepdims=False))
    mine_half = jnp.stack(picked, axis=1)
    other_half = lax.ppermute(mine_half, "core", [(0, 1), (1, 0)])
    blocks = jnp.where(
        my_core == 0,
        jnp.concatenate([mine_half, other_half], axis=2),
        jnp.concatenate([other_half, mine_half], axis=2),
    )
    x = blocks.reshape(n_win, STEPS * rows, nt)

    mine = lax.dynamic_index_in_dim(got, my_core, axis=1, keepdims=False)
    rcv_all = mine[:, :, nt:nt + per].reshape(n_win, half * per)[:, :nt]
    padded = jnp.pad(
        rcv_all.astype(jnp.float32), ((0, 0), (HALF + 1, cols - HALF - 1))
    )[:, None, :]

    out = correlate(x, padded, lag_count, scale)
    return out.reshape(STEPS, rows, 1, lag_count)


def solution(mesh):
    n_chan = mesh.shape["chan"]
    devices = mesh.devices.reshape(mesh.shape["win"], n_chan // 2, 2)
    sub = Mesh(devices, ("win", "zz", "core"))
    chan = ("zz", "core")
    placed = (P("win", chan, None), P("win", chan, None), P(), P(chan), P(chan))
    return jax.shard_map(
        body, mesh=sub, in_specs=placed, out_specs=P(None, "win", chan, None), check_vma=False
    )
```

```python
import functools
import math

import jax
import jax.numpy as jnp
from jax import lax
from jax.experimental import pallas as pl
from jax.experimental.pallas import tpu as pltpu
from jax.sharding import Mesh, PartitionSpec as P

HALF = 750
STEPS = 4
CHUNK = 256

epsilon_energy = 1e-06


def spectral_flatten(traces):
    row_entries, length = traces.shape
    values = traces.astype(jnp.float32).reshape(row_entries, length // 64, 64)
    power = jnp.mean(values * values, axis=-1, keepdims=True)
    return (values * lax.rsqrt(power + epsilon_energy)).reshape(row_entries, length)


def corr_kernel(xa_ref, xb_ref, p_ref, o_ref, *, nt, cols, lags, scale):
    n_win, m, split = xa_ref.shape
    width = CHUNK + cols
    acc = jnp.zeros((m, cols), jnp.float32)
    for w in range(n_win):
        for i in range(nt // CHUNK):
            t0 = i * CHUNK
            start = nt - CHUNK - t0
            v = p_ref[w, :, start:start + width]
            rows = jnp.broadcast_to(v, (CHUNK, width))
            rolled = pltpu.roll(rows, 0, 1, stride=1, stride_axis=0)
            band = rolled[:, CHUNK:CHUNK + cols].astype(jnp.bfloat16)
            if t0 < split:
                lhs = xa_ref[w, :, t0:t0 + CHUNK]
            else:
                lhs = xb_ref[w, :, t0 - split:t0 - split + CHUNK]
            acc = acc + jnp.dot(lhs, band, preferred_element_type=jnp.float32)
    o_ref[...] = (acc * scale)[:, :lags]


def correlate(xa, xb, p, lags, scale):
    n_win, m, split = xa.shape
    nt = split + xb.shape[-1]
    cols = p.shape[-1] - nt
    kern = functools.partial(corr_kernel, nt=nt, cols=cols, lags=lags, scale=scale)
    return pl.pallas_call(
        kern,
        out_shape=jax.ShapeDtypeStruct((m, lags), jnp.float32),
        compiler_params=pltpu.CompilerParams(vmem_limit_bytes=48 * 1024 * 1024),
    )(xa, xb, p)


def body(source_traces, receiver_traces, owners, source_alive, receiver_alive):
    lag_count = 2 * HALF + 1
    n_win = lax.axis_size("win")
    n_core = lax.axis_size("core")
    nt = source_traces.shape[2]
    rows = source_traces.shape[1] // n_win
    half = rows // n_core
    cols = -(-lag_count // 128) * 128
    per = -(-nt // half)
    extra = -(-per // 128) * 128
    scale = 1.0 / math.sqrt(n_win * nt)

    own_white = (
        spectral_flatten(source_traces[0]) * source_alive.astype(jnp.float32)[:, None]
    ).astype(jnp.bfloat16)
    own_white = own_white[:, ::-1].reshape(n_win * n_core, half, nt)
    rcv_white = (
        spectral_flatten(receiver_traces[0]) * receiver_alive.astype(jnp.float32)[:, None]
    ).astype(jnp.bfloat16)
    rcv_rows = jnp.pad(rcv_white.reshape(-1), (0, half * per - nt)).reshape(half, per)
    rcv_rows = jnp.pad(rcv_rows, ((0, 0), (0, extra - per)))
    split = nt // 2 // CHUNK * CHUNK
    pieces = [own_white[:, :, :split], own_white[:, :, split:]]
    pieces[1] = jnp.concatenate(
        [pieces[1], jnp.broadcast_to(rcv_rows, (n_win * n_core, half, extra))], axis=2
    )
    my_core = lax.axis_index("core")
    my_chip = lax.axis_index("zz")
    n_chip = lax.axis_size("zz")
    halves = []
    for h, payload in enumerate(pieces):
        got = lax.all_to_all(payload, ("win", "core"), 0, 0, tiled=True)
        got = got.reshape(n_win, n_core, half, payload.shape[-1])
        if h == 1:
            mine = lax.dynamic_index_in_dim(got, my_core, axis=1, keepdims=False)
            rcv_all = mine[:, :, nt - split:nt - split + per].reshape(n_win, half * per)[:, :nt]
            got = got[..., :nt - split]
        ring = [got] + [
            lax.ppermute(got, "zz", [(i, (i + j) % n_chip) for i in range(n_chip)])
            for j in range(1, n_chip)
        ]
        ring = jnp.stack(ring)
        picked = []
        for k in range(STEPS):
            chip = owners[k] // n_core
            core = owners[k] % n_core
            at = lax.rem(my_chip - chip + n_chip, n_chip)
            block = lax.dynamic_index_in_dim(ring, at, 0, keepdims=False)
            picked.append(lax.dynamic_index_in_dim(block, core, 1, keepdims=False))
        mine_half = jnp.stack(picked, axis=1)
        other_half = lax.ppermute(mine_half, "core", [(0, 1), (1, 0)])
        blocks = jnp.where(
            my_core == 0,
            jnp.concatenate([mine_half, other_half], axis=2),
            jnp.concatenate([other_half, mine_half], axis=2),
        )
        halves.append(blocks.reshape(n_win, STEPS * rows, blocks.shape[-1]))

    padded = jnp.pad(
        rcv_all.astype(jnp.float32), ((0, 0), (HALF + 1, cols - HALF - 1))
    )[:, None, :]

    out = correlate(halves[0], halves[1], padded, lag_count, scale)
    return out.reshape(STEPS, rows, 1, lag_count)


def solution(mesh):
    n_chan = mesh.shape["chan"]
    devices = mesh.devices.reshape(mesh.shape["win"], n_chan // 2, 2)
    sub = Mesh(devices, ("win", "zz", "core"))
    chan = ("zz", "core")
    placed = (P("win", chan, None), P("win", chan, None), P(), P(chan), P(chan))
    return jax.shard_map(
        body, mesh=sub, in_specs=placed, out_specs=P(None, "win", chan, None), check_vma=False
    )
```

```python
import functools
import math

import jax
import jax.numpy as jnp
from jax import lax
from jax.experimental import pallas as pl
from jax.experimental.pallas import tpu as pltpu
from jax.sharding import Mesh, PartitionSpec as P

HALF = 750
STEPS = 4
CHUNK = 256

epsilon_energy = 1e-06


def spectral_flatten(traces):
    row_entries, length = traces.shape
    values = traces.astype(jnp.float32).reshape(row_entries, length // 64, 64)
    power = jnp.mean(values * values, axis=-1, keepdims=True)
    return (values * lax.rsqrt(power + epsilon_energy)).reshape(row_entries, length)


def corr_kernel(x_ref, p_ref, o_ref, *, nt, cols, lags, scale):
    n_win, m, _ = x_ref.shape
    width = CHUNK + cols
    acc = jnp.zeros((m, cols), jnp.float32)
    for w in range(n_win):
        for i in range(nt // CHUNK):
            t0 = i * CHUNK
            start = nt - CHUNK - t0
            v = p_ref[w, :, start:start + width]
            rows = jnp.broadcast_to(v, (CHUNK, width))
            rolled = pltpu.roll(rows, 0, 1, stride=1, stride_axis=0)
            band = rolled[:, CHUNK:CHUNK + cols].astype(jnp.bfloat16)
            acc = acc + jnp.dot(
                x_ref[w, :, t0:t0 + CHUNK], band, preferred_element_type=jnp.float32
            )
    o_ref[...] = (acc * scale)[:, :lags]


def correlate(x, p, lags, scale):
    n_win, m, nt = x.shape
    cols = p.shape[-1] - nt
    kern = functools.partial(corr_kernel, nt=nt, cols=cols, lags=lags, scale=scale)
    return pl.pallas_call(
        kern,
        out_shape=jax.ShapeDtypeStruct((m, lags), jnp.float32),
        compiler_params=pltpu.CompilerParams(vmem_limit_bytes=48 * 1024 * 1024),
    )(x, p)


def body(source_traces, receiver_traces, owners, source_alive, receiver_alive):
    lag_count = 2 * HALF + 1
    n_win = lax.axis_size("win")
    n_core = lax.axis_size("core")
    nt = source_traces.shape[2]
    rows = source_traces.shape[1] // n_win
    half = rows // n_core
    cols = -(-lag_count // 128) * 128
    per = -(-nt // half)
    extra = -(-per // 128) * 128
    scale = 1.0 / math.sqrt(n_win * nt)

    own_white = (
        spectral_flatten(source_traces[0]) * source_alive.astype(jnp.float32)[:, None]
    ).astype(jnp.bfloat16)
    own_white = own_white[:, ::-1].reshape(n_win * n_core, half, nt)
    rcv_white = (
        spectral_flatten(receiver_traces[0]) * receiver_alive.astype(jnp.float32)[:, None]
    ).astype(jnp.bfloat16)
    rcv_rows = jnp.pad(rcv_white.reshape(-1), (0, half * per - nt)).reshape(half, per)
    rcv_rows = jnp.pad(rcv_rows, ((0, 0), (0, extra - per)))
    payload = jnp.concatenate(
        [own_white, jnp.broadcast_to(rcv_rows, (n_win * n_core, half, extra))], axis=2
    )
    got = lax.all_to_all(payload, ("win", "core"), 0, 0, tiled=True)
    got = got.reshape(n_win, n_core, half, nt + extra)

    my_core = lax.axis_index("core")
    my_chip = lax.axis_index("zz")
    n_chip = lax.axis_size("zz")
    src = got[..., :nt]
    chip_of = owners // n_core
    core_of = owners % n_core
    cores = jnp.arange(n_core, dtype=owners.dtype)
    chips = jnp.arange(n_chip, dtype=owners.dtype)
    wanted = jnp.any(
        (chip_of[:, None, None] == chips[None, :, None])
        & (core_of[:, None, None] == cores[None, None, :]),
        axis=0,
    )
    one_slot = jnp.all(jnp.sum(wanted.astype(jnp.int32), axis=1) <= 1)

    def ring_of(part):
        return jnp.stack([part] + [
            lax.ppermute(part, "zz", [(i, (i + j) % n_chip) for i in range(n_chip)])
            for j in range(1, n_chip)
        ])

    def steps_from(ring, pick_core):
        picked = []
        for k in range(STEPS):
            at = lax.rem(my_chip - chip_of[k] + n_chip, n_chip)
            block = lax.dynamic_index_in_dim(ring, at, 0, keepdims=False)
            if pick_core:
                block = lax.dynamic_index_in_dim(block, core_of[k], 1, keepdims=False)
            picked.append(block)
        return jnp.stack(picked, axis=1)

    def both_blocks(src):
        return steps_from(ring_of(src), True)

    def one_block(src):
        slot = jnp.argmax(wanted[my_chip]).astype(jnp.int32)
        part = lax.dynamic_index_in_dim(src, slot, 1, keepdims=False)
        return steps_from(ring_of(part), False)

    mine_half = lax.cond(one_slot, one_block, both_blocks, src)
    other_half = lax.ppermute(mine_half, "core", [(0, 1), (1, 0)])
    blocks = jnp.where(
        my_core == 0,
        jnp.concatenate([mine_half, other_half], axis=2),
        jnp.concatenate([other_half, mine_half], axis=2),
    )
    x = blocks.reshape(n_win, STEPS * rows, nt)

    mine = lax.dynamic_index_in_dim(got, my_core, axis=1, keepdims=False)
    rcv_all = mine[:, :, nt:nt + per].reshape(n_win, half * per)[:, :nt]
    padded = jnp.pad(
        rcv_all.astype(jnp.float32), ((0, 0), (HALF + 1, cols - HALF - 1))
    )[:, None, :]

    out = correlate(x, padded, lag_count, scale)
    return out.reshape(STEPS, rows, 1, lag_count)


def solution(mesh):
    n_chan = mesh.shape["chan"]
    devices = mesh.devices.reshape(mesh.shape["win"], n_chan // 2, 2)
    sub = Mesh(devices, ("win", "zz", "core"))
    chan = ("zz", "core")
    placed = (P("win", chan, None), P("win", chan, None), P(), P(chan), P(chan))
    return jax.shard_map(
        body, mesh=sub, in_specs=placed, out_specs=P(None, "win", chan, None), check_vma=False
    )
```

```python
import functools
import math

import jax
import jax.numpy as jnp
from jax import lax
from jax.experimental import pallas as pl
from jax.experimental.pallas import tpu as pltpu
from jax.sharding import Mesh, PartitionSpec as P

HALF = 750
STEPS = 4
CHUNK = 256

epsilon_energy = 1e-06


def spectral_flatten(traces):
    row_entries, length = traces.shape
    values = traces.astype(jnp.float32).reshape(row_entries, length // 64, 64)
    power = jnp.mean(values * values, axis=-1, keepdims=True)
    return (values * lax.rsqrt(power + epsilon_energy)).reshape(row_entries, length)


def corr_kernel(x_ref, p_ref, o_ref, *, nt, cols, lags, scale):
    n_win, m, _ = x_ref.shape
    width = CHUNK + cols
    acc = jnp.zeros((m, cols), jnp.float32)
    for w in range(n_win):
        for i in range(nt // CHUNK):
            t0 = i * CHUNK
            start = nt - CHUNK - t0
            v = p_ref[w, :, start:start + width]
            rows = jnp.broadcast_to(v, (CHUNK, width))
            rolled = pltpu.roll(rows, 0, 1, stride=1, stride_axis=0)
            band = rolled[:, CHUNK:CHUNK + cols].astype(jnp.bfloat16)
            acc = acc + jnp.dot(
                x_ref[w, :, t0:t0 + CHUNK], band, preferred_element_type=jnp.float32
            )
    o_ref[...] = (acc * scale)[:, :lags]


def correlate(x, p, lags, scale):
    n_win, m, nt = x.shape
    cols = p.shape[-1] - nt
    kern = functools.partial(corr_kernel, nt=nt, cols=cols, lags=lags, scale=scale)
    return pl.pallas_call(
        kern,
        out_shape=jax.ShapeDtypeStruct((m, lags), jnp.float32),
        compiler_params=pltpu.CompilerParams(vmem_limit_bytes=48 * 1024 * 1024),
    )(x, p)


def body(source_traces, receiver_traces, owners, source_alive, receiver_alive):
    lag_count = 2 * HALF + 1
    n_win = lax.axis_size("win")
    n_core = lax.axis_size("core")
    nt = source_traces.shape[2]
    rows = source_traces.shape[1] // n_win
    half = rows // n_core
    cols = -(-lag_count // 128) * 128
    per = -(-nt // half)
    extra = -(-per // 128) * 128
    scale = 1.0 / math.sqrt(n_win * nt)

    own_white = (
        spectral_flatten(source_traces[0]) * source_alive.astype(jnp.float32)[:, None]
    ).astype(jnp.bfloat16)
    own_white = own_white[:, ::-1].reshape(n_win * n_core, half, nt)
    rcv_white = (
        spectral_flatten(receiver_traces[0]) * receiver_alive.astype(jnp.float32)[:, None]
    ).astype(jnp.bfloat16)
    rcv_rows = jnp.pad(rcv_white.reshape(-1), (0, half * per - nt)).reshape(half, per)
    rcv_rows = jnp.pad(rcv_rows, ((0, 0), (0, extra - per)))
    payload = jnp.concatenate(
        [own_white, jnp.broadcast_to(rcv_rows, (n_win * n_core, half, extra))], axis=2
    )
    got = lax.all_to_all(payload, ("win", "core"), 0, 0, tiled=True)
    got = got.reshape(n_win, n_core, half, nt + extra)

    my_core = lax.axis_index("core")
    my_chip = lax.axis_index("zz")
    n_chip = lax.axis_size("zz")
    src = got[..., :nt]
    chip_of = owners // n_core
    core_of = owners % n_core
    cores = jnp.arange(n_core, dtype=owners.dtype)
    chips = jnp.arange(n_chip, dtype=owners.dtype)
    wanted = jnp.any(
        (chip_of[:, None, None] == chips[None, :, None])
        & (core_of[:, None, None] == cores[None, None, :]),
        axis=0,
    )

    def ring_of(part):
        return jnp.stack([part] + [
            lax.ppermute(part, "zz", [(i, (i + j) % n_chip) for i in range(n_chip)])
            for j in range(1, n_chip)
        ])

    def steps_from(ring, pick_core):
        picked = []
        for k in range(STEPS):
            at = lax.rem(my_chip - chip_of[k] + n_chip, n_chip)
            block = lax.dynamic_index_in_dim(ring, at, 0, keepdims=False)
            if pick_core:
                block = lax.dynamic_index_in_dim(block, core_of[k], 1, keepdims=False)
            picked.append(block)
        return jnp.stack(picked, axis=1)

    def both_blocks(src):
        return steps_from(ring_of(src), True)

    def one_block(src):
        slot = jnp.argmax(wanted[my_chip]).astype(jnp.int32)
        part = lax.dynamic_index_in_dim(src, slot, 1, keepdims=False)
        return steps_from(ring_of(part), False)

    def one_double(c):
        def run(src):
            slot = jnp.argmax(wanted[my_chip]).astype(jnp.int32)
            part = lax.dynamic_index_in_dim(src, slot, 1, keepdims=False)
            first = steps_from(ring_of(part), False)
            extra = src[:, n_core - 1]
            second = jnp.where(my_chip == c, extra, jnp.zeros_like(extra))
            for j in range(1, n_chip):
                second = second + lax.ppermute(extra, "zz", [(c, (c + j) % n_chip)])
            late = owners == c * n_core + n_core - 1
            return jnp.where(late[None, :, None, None], second[:, None], first)
        return run

    doubles = jnp.sum(wanted.astype(jnp.int32), axis=1) == n_core
    n_doubles = jnp.sum(doubles.astype(jnp.int32))
    if n_chip <= 4 and n_core == 2:
        which = jnp.where(
            n_doubles == 0, 0,
            jnp.where(n_doubles == 1, 1 + jnp.argmax(doubles).astype(jnp.int32), n_chip + 1),
        )
        branches = [one_block] + [one_double(c) for c in range(n_chip)] + [both_blocks]
        mine_half = lax.switch(which, branches, src)
    else:
        mine_half = lax.cond(n_doubles == 0, one_block, both_blocks, src)
    other_half = lax.ppermute(mine_half, "core", [(0, 1), (1, 0)])
    blocks = jnp.where(
        my_core == 0,
        jnp.concatenate([mine_half, other_half], axis=2),
        jnp.concatenate([other_half, mine_half], axis=2),
    )
    x = blocks.reshape(n_win, STEPS * rows, nt)

    mine = lax.dynamic_index_in_dim(got, my_core, axis=1, keepdims=False)
    rcv_all = mine[:, :, nt:nt + per].reshape(n_win, half * per)[:, :nt]
    padded = jnp.pad(
        rcv_all.astype(jnp.float32), ((0, 0), (HALF + 1, cols - HALF - 1))
    )[:, None, :]

    out = correlate(x, padded, lag_count, scale)
    return out.reshape(STEPS, rows, 1, lag_count)


def solution(mesh):
    n_chan = mesh.shape["chan"]
    devices = mesh.devices.reshape(mesh.shape["win"], n_chan // 2, 2)
    sub = Mesh(devices, ("win", "zz", "core"))
    chan = ("zz", "core")
    placed = (P("win", chan, None), P("win", chan, None), P(), P(chan), P(chan))
    return jax.shard_map(
        body, mesh=sub, in_specs=placed, out_specs=P(None, "win", chan, None), check_vma=False
    )
```

```python
import functools
import math

import jax
import jax.numpy as jnp
from jax import lax
from jax.experimental import pallas as pl
from jax.experimental.pallas import tpu as pltpu
from jax.sharding import Mesh, PartitionSpec as P

HALF = 750
STEPS = 4
CHUNK = 256

epsilon_energy = 1e-06


def spectral_flatten(traces):
    row_entries, length = traces.shape
    values = traces.astype(jnp.float32).reshape(row_entries, length // 64, 64)
    power = jnp.mean(values * values, axis=-1, keepdims=True)
    return (values * lax.rsqrt(power + epsilon_energy)).reshape(row_entries, length)


def corr_kernel(x_ref, p_ref, o_ref, *, nt, cols, lags, scale):
    n_win, m, _ = x_ref.shape
    width = CHUNK + cols
    acc = jnp.zeros((m, cols), jnp.float32)
    row = lax.broadcasted_iota(jnp.int32, (CHUNK, CHUNK), 0)
    col = lax.broadcasted_iota(jnp.int32, (CHUNK, CHUNK), 1)
    flip = (row + col == CHUNK - 1).astype(jnp.bfloat16)
    for w in range(n_win):
        for i in range(nt // CHUNK):
            t0 = i * CHUNK
            start = nt - CHUNK - t0
            v = p_ref[w, :, start:start + width]
            rows = jnp.broadcast_to(v, (CHUNK, width))
            rolled = pltpu.roll(rows, 0, 1, stride=1, stride_axis=0)
            band = rolled[:, CHUNK:CHUNK + cols].astype(jnp.bfloat16)
            s0 = nt - CHUNK - t0
            lhs = jnp.dot(
                x_ref[w, :, s0:s0 + CHUNK], flip, preferred_element_type=jnp.float32
            ).astype(jnp.bfloat16)
            acc = acc + jnp.dot(lhs, band, preferred_element_type=jnp.float32)
    o_ref[...] = (acc * scale)[:, :lags]


def correlate(x, p, lags, scale):
    n_win, m, nt = x.shape
    cols = p.shape[-1] - nt
    kern = functools.partial(corr_kernel, nt=nt, cols=cols, lags=lags, scale=scale)
    return pl.pallas_call(
        kern,
        out_shape=jax.ShapeDtypeStruct((m, lags), jnp.float32),
        compiler_params=pltpu.CompilerParams(vmem_limit_bytes=48 * 1024 * 1024),
    )(x, p)


def body(source_traces, receiver_traces, owners, source_alive, receiver_alive):
    lag_count = 2 * HALF + 1
    n_win = lax.axis_size("win")
    n_core = lax.axis_size("core")
    nt = source_traces.shape[2]
    rows = source_traces.shape[1] // n_win
    half = rows // n_core
    cols = -(-lag_count // 128) * 128
    per = -(-nt // half)
    extra = -(-per // 128) * 128
    scale = 1.0 / math.sqrt(n_win * nt)

    own_white = (
        spectral_flatten(source_traces[0]) * source_alive.astype(jnp.float32)[:, None]
    ).astype(jnp.bfloat16)
    own_white = own_white.reshape(n_win * n_core, half, nt)
    rcv_white = (
        spectral_flatten(receiver_traces[0]) * receiver_alive.astype(jnp.float32)[:, None]
    ).astype(jnp.bfloat16)
    rcv_rows = jnp.pad(rcv_white.reshape(-1), (0, half * per - nt)).reshape(half, per)
    rcv_rows = jnp.pad(rcv_rows, ((0, 0), (0, extra - per)))
    payload = jnp.concatenate(
        [own_white, jnp.broadcast_to(rcv_rows, (n_win * n_core, half, extra))], axis=2
    )
    got = lax.all_to_all(payload, ("win", "core"), 0, 0, tiled=True)
    got = got.reshape(n_win, n_core, half, nt + extra)

    my_core = lax.axis_index("core")
    my_chip = lax.axis_index("zz")
    n_chip = lax.axis_size("zz")
    src = got[..., :nt]
    chip_of = owners // n_core
    core_of = owners % n_core
    cores = jnp.arange(n_core, dtype=owners.dtype)
    chips = jnp.arange(n_chip, dtype=owners.dtype)
    wanted = jnp.any(
        (chip_of[:, None, None] == chips[None, :, None])
        & (core_of[:, None, None] == cores[None, None, :]),
        axis=0,
    )

    def ring_of(part):
        return jnp.stack([part] + [
            lax.ppermute(part, "zz", [(i, (i + j) % n_chip) for i in range(n_chip)])
            for j in range(1, n_chip)
        ])

    def steps_from(ring, pick_core):
        picked = []
        for k in range(STEPS):
            at = lax.rem(my_chip - chip_of[k] + n_chip, n_chip)
            block = lax.dynamic_index_in_dim(ring, at, 0, keepdims=False)
            if pick_core:
                block = lax.dynamic_index_in_dim(block, core_of[k], 1, keepdims=False)
            picked.append(block)
        return jnp.stack(picked, axis=1)

    def both_blocks(src):
        return steps_from(ring_of(src), True)

    def one_block(src):
        slot = jnp.argmax(wanted[my_chip]).astype(jnp.int32)
        part = lax.dynamic_index_in_dim(src, slot, 1, keepdims=False)
        return steps_from(ring_of(part), False)

    def one_double(c):
        def run(src):
            slot = jnp.argmax(wanted[my_chip]).astype(jnp.int32)
            part = lax.dynamic_index_in_dim(src, slot, 1, keepdims=False)
            first = steps_from(ring_of(part), False)
            extra = src[:, n_core - 1]
            second = jnp.where(my_chip == c, extra, jnp.zeros_like(extra))
            for j in range(1, n_chip):
                second = second + lax.ppermute(extra, "zz", [(c, (c + j) % n_chip)])
            late = owners == c * n_core + n_core - 1
            return jnp.where(late[None, :, None, None], second[:, None], first)
        return run

    doubles = jnp.sum(wanted.astype(jnp.int32), axis=1) == n_core
    n_doubles = jnp.sum(doubles.astype(jnp.int32))
    if n_chip <= 4 and n_core == 2:
        which = jnp.where(
            n_doubles == 0, 0,
            jnp.where(n_doubles == 1, 1 + jnp.argmax(doubles).astype(jnp.int32), n_chip + 1),
        )
        branches = [one_block] + [one_double(c) for c in range(n_chip)] + [both_blocks]
        mine_half = lax.switch(which, branches, src)
    else:
        mine_half = lax.cond(n_doubles == 0, one_block, both_blocks, src)
    other_half = lax.ppermute(mine_half, "core", [(0, 1), (1, 0)])
    blocks = jnp.where(
        my_core == 0,
        jnp.concatenate([mine_half, other_half], axis=2),
        jnp.concatenate([other_half, mine_half], axis=2),
    )
    x = blocks.reshape(n_win, STEPS * rows, nt)

    mine = lax.dynamic_index_in_dim(got, my_core, axis=1, keepdims=False)
    rcv_all = mine[:, :, nt:nt + per].reshape(n_win, half * per)[:, :nt]
    padded = jnp.pad(
        rcv_all.astype(jnp.float32), ((0, 0), (HALF + 1, cols - HALF - 1))
    )[:, None, :]

    out = correlate(x, padded, lag_count, scale)
    return out.reshape(STEPS, rows, 1, lag_count)


def solution(mesh):
    n_chan = mesh.shape["chan"]
    devices = mesh.devices.reshape(mesh.shape["win"], n_chan // 2, 2)
    sub = Mesh(devices, ("win", "zz", "core"))
    chan = ("zz", "core")
    placed = (P("win", chan, None), P("win", chan, None), P(), P(chan), P(chan))
    return jax.shard_map(
        body, mesh=sub, in_specs=placed, out_specs=P(None, "win", chan, None), check_vma=False
    )
```

```python
import functools
import math

import jax
import jax.numpy as jnp
from jax import lax
from jax.experimental import pallas as pl
from jax.experimental.pallas import tpu as pltpu
from jax.sharding import Mesh, PartitionSpec as P

HALF = 750
STEPS = 4
CHUNK = 256

epsilon_energy = 1e-06


def spectral_flatten(traces):
    row_entries, length = traces.shape
    values = traces.astype(jnp.float32).reshape(row_entries, length // 64, 64)
    power = jnp.mean(values * values, axis=-1, keepdims=True)
    return (values * lax.rsqrt(power + epsilon_energy)).reshape(row_entries, length)


def corr_kernel(x_ref, p_ref, o_ref, *, nt, cols, lags, scale):
    n_win, m, _ = x_ref.shape
    width = CHUNK + cols
    acc = jnp.zeros((m, cols), jnp.float32)
    for w in range(n_win):
        for i in range(nt // CHUNK):
            t0 = i * CHUNK
            start = nt - CHUNK - t0
            v = p_ref[w, :, start:start + width]
            rows = jnp.broadcast_to(v, (CHUNK, width))
            rolled = pltpu.roll(rows, 0, 1, stride=1, stride_axis=0)
            band = rolled[:, CHUNK:CHUNK + cols].astype(jnp.bfloat16)
            acc = acc + jnp.dot(
                x_ref[w, :, t0:t0 + CHUNK], band, preferred_element_type=jnp.float32
            )
    o_ref[...] = (acc * scale)[:, :lags]


def correlate(x, p, lags, scale):
    n_win, m, nt = x.shape
    cols = p.shape[-1] - nt
    kern = functools.partial(corr_kernel, nt=nt, cols=cols, lags=lags, scale=scale)
    return pl.pallas_call(
        kern,
        out_shape=jax.ShapeDtypeStruct((m, lags), jnp.float32),
        compiler_params=pltpu.CompilerParams(vmem_limit_bytes=48 * 1024 * 1024),
    )(x, p)


def front_kernel(x_ref, al_ref, r_ref, o_ref, *, nt):
    x = x_ref[0].astype(jnp.float32)
    n_rows = x.shape[0]
    runs = nt // 64
    hi = lax.Precision.HIGHEST
    t_run = lax.broadcasted_iota(jnp.int32, (nt, runs), 0) // 64
    run_of = (t_run == lax.broadcasted_iota(jnp.int32, (nt, runs), 1)).astype(jnp.float32)
    sums = jnp.dot(x * x, run_of, precision=hi, preferred_element_type=jnp.float32)
    gain = lax.rsqrt(sums / 64.0 + epsilon_energy)
    r_run = lax.broadcasted_iota(jnp.int32, (runs, nt), 1) // 64
    spread = (r_run == lax.broadcasted_iota(jnp.int32, (runs, nt), 0)).astype(jnp.float32)
    gain_t = jnp.dot(gain, spread, precision=hi, preferred_element_type=jnp.float32)
    eye = (
        lax.broadcasted_iota(jnp.int32, (n_rows, n_rows), 0)
        == lax.broadcasted_iota(jnp.int32, (n_rows, n_rows), 1)
    ).astype(jnp.float32)
    alive = al_ref[...].astype(jnp.float32)
    alive_col = jnp.dot(eye * alive, jnp.ones((n_rows, 128), jnp.float32),
                        preferred_element_type=jnp.float32)[:, :1]
    white = (x * gain_t * alive_col).astype(jnp.bfloat16)
    row = lax.broadcasted_iota(jnp.int32, (CHUNK, CHUNK), 0)
    col = lax.broadcasted_iota(jnp.int32, (CHUNK, CHUNK), 1)
    flip = (row + col == CHUNK - 1).astype(jnp.bfloat16)
    pieces = []
    for i in range(nt // CHUNK):
        s0 = nt - CHUNK * (i + 1)
        pieces.append(jnp.dot(white[:, s0:s0 + CHUNK], flip,
                              preferred_element_type=jnp.float32).astype(jnp.bfloat16))
    rev = jnp.concatenate(pieces, axis=1)
    n_out, half, _ = o_ref.shape
    for j in range(n_out):
        o_ref[j, :, :nt] = rev[j * half:(j + 1) * half]
        o_ref[j, :, nt:] = r_ref[...]


def front(source_traces, source_alive, rcv_rows, n_out):
    _, n_rows, nt = source_traces.shape
    half, extra = rcv_rows.shape
    kern = functools.partial(front_kernel, nt=nt)
    return pl.pallas_call(
        kern,
        out_shape=jax.ShapeDtypeStruct((n_out, half, nt + extra), jnp.bfloat16),
    )(source_traces, source_alive.reshape(1, n_rows), rcv_rows)


def body(source_traces, receiver_traces, owners, source_alive, receiver_alive):
    lag_count = 2 * HALF + 1
    n_win = lax.axis_size("win")
    n_core = lax.axis_size("core")
    nt = source_traces.shape[2]
    rows = source_traces.shape[1] // n_win
    half = rows // n_core
    cols = -(-lag_count // 128) * 128
    per = -(-nt // half)
    extra = -(-per // 128) * 128
    scale = 1.0 / math.sqrt(n_win * nt)

    rcv_white = (
        spectral_flatten(receiver_traces[0]) * receiver_alive.astype(jnp.float32)[:, None]
    ).astype(jnp.bfloat16)
    rcv_rows = jnp.pad(rcv_white.reshape(-1), (0, half * per - nt)).reshape(half, per)
    rcv_rows = jnp.pad(rcv_rows, ((0, 0), (0, extra - per)))
    payload = front(source_traces, source_alive, rcv_rows, n_win * n_core)
    got = lax.all_to_all(payload, ("win", "core"), 0, 0, tiled=True)
    got = got.reshape(n_win, n_core, half, nt + extra)

    my_core = lax.axis_index("core")
    my_chip = lax.axis_index("zz")
    n_chip = lax.axis_size("zz")
    src = got[..., :nt]
    chip_of = owners // n_core
    core_of = owners % n_core
    cores = jnp.arange(n_core, dtype=owners.dtype)
    chips = jnp.arange(n_chip, dtype=owners.dtype)
    wanted = jnp.any(
        (chip_of[:, None, None] == chips[None, :, None])
        & (core_of[:, None, None] == cores[None, None, :]),
        axis=0,
    )

    def ring_of(part):
        return jnp.stack([part] + [
            lax.ppermute(part, "zz", [(i, (i + j) % n_chip) for i in range(n_chip)])
            for j in range(1, n_chip)
        ])

    def steps_from(ring, pick_core):
        picked = []
        for k in range(STEPS):
            at = lax.rem(my_chip - chip_of[k] + n_chip, n_chip)
            block = lax.dynamic_index_in_dim(ring, at, 0, keepdims=False)
            if pick_core:
                block = lax.dynamic_index_in_dim(block, core_of[k], 1, keepdims=False)
            picked.append(block)
        return jnp.stack(picked, axis=1)

    def both_blocks(src):
        return steps_from(ring_of(src), True)

    def one_block(src):
        slot = jnp.argmax(wanted[my_chip]).astype(jnp.int32)
        part = lax.dynamic_index_in_dim(src, slot, 1, keepdims=False)
        return steps_from(ring_of(part), False)

    def one_double(c):
        def run(src):
            slot = jnp.argmax(wanted[my_chip]).astype(jnp.int32)
            part = lax.dynamic_index_in_dim(src, slot, 1, keepdims=False)
            first = steps_from(ring_of(part), False)
            extra = src[:, n_core - 1]
            second = jnp.where(my_chip == c, extra, jnp.zeros_like(extra))
            for j in range(1, n_chip):
                second = second + lax.ppermute(extra, "zz", [(c, (c + j) % n_chip)])
            late = owners == c * n_core + n_core - 1
            return jnp.where(late[None, :, None, None], second[:, None], first)
        return run

    doubles = jnp.sum(wanted.astype(jnp.int32), axis=1) == n_core
    n_doubles = jnp.sum(doubles.astype(jnp.int32))
    if n_chip <= 4 and n_core == 2:
        which = jnp.where(
            n_doubles == 0, 0,
            jnp.where(n_doubles == 1, 1 + jnp.argmax(doubles).astype(jnp.int32), n_chip + 1),
        )
        branches = [one_block] + [one_double(c) for c in range(n_chip)] + [both_blocks]
        mine_half = lax.switch(which, branches, src)
    else:
        mine_half = lax.cond(n_doubles == 0, one_block, both_blocks, src)
    other_half = lax.ppermute(mine_half, "core", [(0, 1), (1, 0)])
    blocks = jnp.where(
        my_core == 0,
        jnp.concatenate([mine_half, other_half], axis=2),
        jnp.concatenate([other_half, mine_half], axis=2),
    )
    x = blocks.reshape(n_win, STEPS * rows, nt)

    mine = lax.dynamic_index_in_dim(got, my_core, axis=1, keepdims=False)
    rcv_all = mine[:, :, nt:nt + per].reshape(n_win, half * per)[:, :nt]
    padded = jnp.pad(
        rcv_all.astype(jnp.float32), ((0, 0), (HALF + 1, cols - HALF - 1))
    )[:, None, :]

    out = correlate(x, padded, lag_count, scale)
    return out.reshape(STEPS, rows, 1, lag_count)


def solution(mesh):
    n_chan = mesh.shape["chan"]
    devices = mesh.devices.reshape(mesh.shape["win"], n_chan // 2, 2)
    sub = Mesh(devices, ("win", "zz", "core"))
    chan = ("zz", "core")
    placed = (P("win", chan, None), P("win", chan, None), P(), P(chan), P(chan))
    return jax.shard_map(
        body, mesh=sub, in_specs=placed, out_specs=P(None, "win", chan, None), check_vma=False
    )
```

```python
import functools
import math

import jax
import jax.numpy as jnp
from jax import lax
from jax.experimental import pallas as pl
from jax.experimental.pallas import tpu as pltpu
from jax.sharding import Mesh, PartitionSpec as P

HALF = 750
STEPS = 4
CHUNK = 256

epsilon_energy = 1e-06


def spectral_flatten(traces):
    row_entries, length = traces.shape
    values = traces.astype(jnp.float32).reshape(row_entries, length // 64, 64)
    power = jnp.mean(values * values, axis=-1, keepdims=True)
    return (values * lax.rsqrt(power + epsilon_energy)).reshape(row_entries, length)


def corr_kernel(x_ref, p_ref, o_ref, *, nt, cols, lags, scale):
    n_win, m, _ = x_ref.shape
    width = CHUNK + cols
    acc = jnp.zeros((m, cols), jnp.float32)
    for w in range(n_win):
        for i in range(nt // CHUNK):
            t0 = i * CHUNK
            start = nt - CHUNK - t0
            v = p_ref[w, :, start:start + width]
            rows = jnp.broadcast_to(v, (CHUNK, width))
            rolled = pltpu.roll(rows, 0, 1, stride=1, stride_axis=0)
            band = rolled[:, CHUNK:CHUNK + cols].astype(jnp.bfloat16)
            acc = acc + jnp.dot(
                x_ref[w, :, t0:t0 + CHUNK], band, preferred_element_type=jnp.float32
            )
    o_ref[...] = (acc * scale)[:, :lags].reshape(m, 1, lags)


def correlate(x, p, lags, scale):
    n_win, m, nt = x.shape
    cols = p.shape[-1] - nt
    kern = functools.partial(corr_kernel, nt=nt, cols=cols, lags=lags, scale=scale)
    return pl.pallas_call(
        kern,
        out_shape=jax.ShapeDtypeStruct((m, 1, lags), jnp.float32),
        compiler_params=pltpu.CompilerParams(vmem_limit_bytes=48 * 1024 * 1024),
    )(x, p)


def body(source_traces, receiver_traces, owners, source_alive, receiver_alive):
    lag_count = 2 * HALF + 1
    n_win = lax.axis_size("win")
    n_core = lax.axis_size("core")
    nt = source_traces.shape[2]
    rows = source_traces.shape[1] // n_win
    half = rows // n_core
    cols = -(-lag_count // 128) * 128
    per = -(-nt // half)
    extra = -(-per // 128) * 128
    scale = 1.0 / math.sqrt(n_win * nt)

    own_white = (
        spectral_flatten(source_traces[0]) * source_alive.astype(jnp.float32)[:, None]
    ).astype(jnp.bfloat16)
    own_white = own_white[:, ::-1].reshape(n_win * n_core, half, nt)
    rcv_white = (
        spectral_flatten(receiver_traces[0]) * receiver_alive.astype(jnp.float32)[:, None]
    ).astype(jnp.bfloat16)
    rcv_rows = jnp.pad(rcv_white.reshape(-1), (0, half * per - nt)).reshape(half, per)
    rcv_rows = jnp.pad(rcv_rows, ((0, 0), (0, extra - per)))
    payload = jnp.concatenate(
        [own_white, jnp.broadcast_to(rcv_rows, (n_win * n_core, half, extra))], axis=2
    )
    got = lax.all_to_all(payload, ("win", "core"), 0, 0, tiled=True)
    got = got.reshape(n_win, n_core, half, nt + extra)

    my_core = lax.axis_index("core")
    my_chip = lax.axis_index("zz")
    n_chip = lax.axis_size("zz")
    src = got[..., :nt]
    chip_of = owners // n_core
    core_of = owners % n_core
    cores = jnp.arange(n_core, dtype=owners.dtype)
    chips = jnp.arange(n_chip, dtype=owners.dtype)
    wanted = jnp.any(
        (chip_of[:, None, None] == chips[None, :, None])
        & (core_of[:, None, None] == cores[None, None, :]),
        axis=0,
    )

    def ring_of(part):
        return jnp.stack([part] + [
            lax.ppermute(part, "zz", [(i, (i + j) % n_chip) for i in range(n_chip)])
            for j in range(1, n_chip)
        ])

    def steps_from(ring, pick_core):
        picked = []
        for k in range(STEPS):
            at = lax.rem(my_chip - chip_of[k] + n_chip, n_chip)
            block = lax.dynamic_index_in_dim(ring, at, 0, keepdims=False)
            if pick_core:
                block = lax.dynamic_index_in_dim(block, core_of[k], 1, keepdims=False)
            picked.append(block)
        return jnp.stack(picked, axis=1)

    def both_blocks(src):
        return steps_from(ring_of(src), True)

    def one_block(src):
        slot = jnp.argmax(wanted[my_chip]).astype(jnp.int32)
        part = lax.dynamic_index_in_dim(src, slot, 1, keepdims=False)
        return steps_from(ring_of(part), False)

    def one_double(c):
        def run(src):
            slot = jnp.argmax(wanted[my_chip]).astype(jnp.int32)
            part = lax.dynamic_index_in_dim(src, slot, 1, keepdims=False)
            first = steps_from(ring_of(part), False)
            extra = src[:, n_core - 1]
            second = jnp.where(my_chip == c, extra, jnp.zeros_like(extra))
            for j in range(1, n_chip):
                second = second + lax.ppermute(extra, "zz", [(c, (c + j) % n_chip)])
            late = owners == c * n_core + n_core - 1
            return jnp.where(late[None, :, None, None], second[:, None], first)
        return run

    doubles = jnp.sum(wanted.astype(jnp.int32), axis=1) == n_core
    n_doubles = jnp.sum(doubles.astype(jnp.int32))
    if n_chip <= 4 and n_core == 2:
        which = jnp.where(
            n_doubles == 0, 0,
            jnp.where(n_doubles == 1, 1 + jnp.argmax(doubles).astype(jnp.int32), n_chip + 1),
        )
        branches = [one_block] + [one_double(c) for c in range(n_chip)] + [both_blocks]
        mine_half = lax.switch(which, branches, src)
    else:
        mine_half = lax.cond(n_doubles == 0, one_block, both_blocks, src)
    other_half = lax.ppermute(mine_half, "core", [(0, 1), (1, 0)])
    blocks = jnp.where(
        my_core == 0,
        jnp.concatenate([mine_half, other_half], axis=2),
        jnp.concatenate([other_half, mine_half], axis=2),
    )
    x = blocks.reshape(n_win, STEPS * rows, nt)

    mine = lax.dynamic_index_in_dim(got, my_core, axis=1, keepdims=False)
    rcv_all = mine[:, :, nt:nt + per].reshape(n_win, half * per)[:, :nt]
    padded = jnp.pad(
        rcv_all.astype(jnp.float32), ((0, 0), (HALF + 1, cols - HALF - 1))
    )[:, None, :]

    out = correlate(x, padded, lag_count, scale)
    return out.reshape(STEPS, rows, 1, lag_count)


def solution(mesh):
    n_chan = mesh.shape["chan"]
    devices = mesh.devices.reshape(mesh.shape["win"], n_chan // 2, 2)
    sub = Mesh(devices, ("win", "zz", "core"))
    chan = ("zz", "core")
    placed = (P("win", chan, None), P("win", chan, None), P(), P(chan), P(chan))
    return jax.shard_map(
        body, mesh=sub, in_specs=placed, out_specs=P(None, "win", chan, None), check_vma=False
    )
```

```python
import functools
import math

import jax
import jax.numpy as jnp
from jax import lax
from jax.experimental import pallas as pl
from jax.experimental.pallas import tpu as pltpu
from jax.sharding import Mesh, PartitionSpec as P

HALF = 750
STEPS = 4
CHUNK = 256

epsilon_energy = 1e-06


def spectral_flatten(traces):
    row_entries, length = traces.shape
    values = traces.astype(jnp.float32).reshape(row_entries, length // 64, 64)
    power = jnp.mean(values * values, axis=-1, keepdims=True)
    return (values * lax.rsqrt(power + epsilon_energy)).reshape(row_entries, length)


def corr_kernel(x_ref, p_ref, o_ref, *, nt, cols, lags, scale):
    n_win, m, _ = x_ref.shape
    width = CHUNK + cols
    acc = jnp.zeros((m, cols), jnp.float32)
    for w in range(n_win):
        for i in range(nt // CHUNK):
            t0 = i * CHUNK
            start = nt - CHUNK - t0
            v = p_ref[w, :, start:start + width]
            rows = jnp.broadcast_to(v, (CHUNK, width))
            rolled = pltpu.roll(rows, 0, 1, stride=1, stride_axis=0)
            band = rolled[:, CHUNK:CHUNK + cols]
            acc = acc + jnp.dot(
                x_ref[w, :, t0:t0 + CHUNK], band, preferred_element_type=jnp.float32
            )
    o_ref[...] = (acc * scale)[:, :lags].reshape(m, 1, lags)


def correlate(x, p, lags, scale):
    n_win, m, nt = x.shape
    cols = p.shape[-1] - nt
    kern = functools.partial(corr_kernel, nt=nt, cols=cols, lags=lags, scale=scale)
    return pl.pallas_call(
        kern,
        out_shape=jax.ShapeDtypeStruct((m, 1, lags), jnp.float32),
        compiler_params=pltpu.CompilerParams(vmem_limit_bytes=48 * 1024 * 1024),
    )(x, p)


def body(source_traces, receiver_traces, owners, source_alive, receiver_alive):
    lag_count = 2 * HALF + 1
    n_win = lax.axis_size("win")
    n_core = lax.axis_size("core")
    nt = source_traces.shape[2]
    rows = source_traces.shape[1] // n_win
    half = rows // n_core
    cols = -(-lag_count // 128) * 128
    per = -(-nt // half)
    extra = -(-per // 128) * 128
    scale = 1.0 / math.sqrt(n_win * nt)

    own_white = (
        spectral_flatten(source_traces[0]) * source_alive.astype(jnp.float32)[:, None]
    ).astype(jnp.bfloat16)
    own_white = own_white[:, ::-1].reshape(n_win * n_core, half, nt)
    rcv_white = (
        spectral_flatten(receiver_traces[0]) * receiver_alive.astype(jnp.float32)[:, None]
    ).astype(jnp.bfloat16)
    rcv_rows = jnp.pad(rcv_white.reshape(-1), (0, half * per - nt)).reshape(half, per)
    rcv_rows = jnp.pad(rcv_rows, ((0, 0), (0, extra - per)))
    payload = jnp.concatenate(
        [own_white, jnp.broadcast_to(rcv_rows, (n_win * n_core, half, extra))], axis=2
    )
    got = lax.all_to_all(payload, ("win", "core"), 0, 0, tiled=True)
    got = got.reshape(n_win, n_core, half, nt + extra)

    my_core = lax.axis_index("core")
    my_chip = lax.axis_index("zz")
    n_chip = lax.axis_size("zz")
    src = got[..., :nt]
    chip_of = owners // n_core
    core_of = owners % n_core
    cores = jnp.arange(n_core, dtype=owners.dtype)
    chips = jnp.arange(n_chip, dtype=owners.dtype)
    wanted = jnp.any(
        (chip_of[:, None, None] == chips[None, :, None])
        & (core_of[:, None, None] == cores[None, None, :]),
        axis=0,
    )

    def ring_of(part):
        return jnp.stack([part] + [
            lax.ppermute(part, "zz", [(i, (i + j) % n_chip) for i in range(n_chip)])
            for j in range(1, n_chip)
        ])

    def steps_from(ring, pick_core):
        picked = []
        for k in range(STEPS):
            at = lax.rem(my_chip - chip_of[k] + n_chip, n_chip)
            block = lax.dynamic_index_in_dim(ring, at, 0, keepdims=False)
            if pick_core:
                block = lax.dynamic_index_in_dim(block, core_of[k], 1, keepdims=False)
            picked.append(block)
        return jnp.stack(picked, axis=1)

    def both_blocks(src):
        return steps_from(ring_of(src), True)

    def one_block(src):
        slot = jnp.argmax(wanted[my_chip]).astype(jnp.int32)
        part = lax.dynamic_index_in_dim(src, slot, 1, keepdims=False)
        return steps_from(ring_of(part), False)

    def one_double(c):
        def run(src):
            slot = jnp.argmax(wanted[my_chip]).astype(jnp.int32)
            part = lax.dynamic_index_in_dim(src, slot, 1, keepdims=False)
            first = steps_from(ring_of(part), False)
            extra = src[:, n_core - 1]
            second = jnp.where(my_chip == c, extra, jnp.zeros_like(extra))
            for j in range(1, n_chip):
                second = second + lax.ppermute(extra, "zz", [(c, (c + j) % n_chip)])
            late = owners == c * n_core + n_core - 1
            return jnp.where(late[None, :, None, None], second[:, None], first)
        return run

    doubles = jnp.sum(wanted.astype(jnp.int32), axis=1) == n_core
    n_doubles = jnp.sum(doubles.astype(jnp.int32))
    if n_chip <= 4 and n_core == 2:
        which = jnp.where(
            n_doubles == 0, 0,
            jnp.where(n_doubles == 1, 1 + jnp.argmax(doubles).astype(jnp.int32), n_chip + 1),
        )
        branches = [one_block] + [one_double(c) for c in range(n_chip)] + [both_blocks]
        mine_half = lax.switch(which, branches, src)
    else:
        mine_half = lax.cond(n_doubles == 0, one_block, both_blocks, src)
    other_half = lax.ppermute(mine_half, "core", [(0, 1), (1, 0)])
    blocks = jnp.where(
        my_core == 0,
        jnp.concatenate([mine_half, other_half], axis=2),
        jnp.concatenate([other_half, mine_half], axis=2),
    )
    x = blocks.reshape(n_win, STEPS * rows, nt)

    mine = lax.dynamic_index_in_dim(got, my_core, axis=1, keepdims=False)
    rcv_all = mine[:, :, nt:nt + per].reshape(n_win, half * per)[:, :nt]
    padded = jnp.pad(
        rcv_all, ((0, 0), (HALF + 1, cols - HALF - 1))
    )[:, None, :]

    out = correlate(x, padded, lag_count, scale)
    return out.reshape(STEPS, rows, 1, lag_count)


def solution(mesh):
    n_chan = mesh.shape["chan"]
    devices = mesh.devices.reshape(mesh.shape["win"], n_chan // 2, 2)
    sub = Mesh(devices, ("win", "zz", "core"))
    chan = ("zz", "core")
    placed = (P("win", chan, None), P("win", chan, None), P(), P(chan), P(chan))
    return jax.shard_map(
        body, mesh=sub, in_specs=placed, out_specs=P(None, "win", chan, None), check_vma=False
    )
```

```python
import functools
import math

import jax
import jax.numpy as jnp
from jax import lax
from jax.experimental import pallas as pl
from jax.experimental.pallas import tpu as pltpu
from jax.sharding import Mesh, PartitionSpec as P

HALF = 750
STEPS = 4
CHUNK = 256

epsilon_energy = 1e-06


def flatten_rows(traces):
    row_entries, length = traces.shape
    values = traces.astype(jnp.float32)
    runs = length // 64
    member = (
        jnp.arange(length, dtype=jnp.int32)[:, None] // 64
        == jnp.arange(runs, dtype=jnp.int32)[None, :]
    ).astype(jnp.float32)
    hi = lax.Precision.HIGHEST
    power = jnp.dot(values * values, member, precision=hi) / 64.0
    gain = jnp.dot(lax.rsqrt(power + epsilon_energy), member.T, precision=hi)
    return values * gain


def spectral_flatten(traces):
    row_entries, length = traces.shape
    values = traces.astype(jnp.float32).reshape(row_entries, length // 64, 64)
    power = jnp.mean(values * values, axis=-1, keepdims=True)
    return (values * lax.rsqrt(power + epsilon_energy)).reshape(row_entries, length)


def corr_kernel(x_ref, p_ref, o_ref, *, nt, cols, lags, scale):
    n_win, m, _ = x_ref.shape
    width = CHUNK + cols
    acc = jnp.zeros((m, cols), jnp.float32)
    for w in range(n_win):
        for i in range(nt // CHUNK):
            t0 = i * CHUNK
            start = nt - CHUNK - t0
            v = p_ref[w, :, start:start + width]
            rows = jnp.broadcast_to(v, (CHUNK, width))
            rolled = pltpu.roll(rows, 0, 1, stride=1, stride_axis=0)
            band = rolled[:, CHUNK:CHUNK + cols]
            acc = acc + jnp.dot(
                x_ref[w, :, t0:t0 + CHUNK], band, preferred_element_type=jnp.float32
            )
    o_ref[...] = (acc * scale)[:, :lags].reshape(m, 1, lags)


def correlate(x, p, lags, scale):
    n_win, m, nt = x.shape
    cols = p.shape[-1] - nt
    kern = functools.partial(corr_kernel, nt=nt, cols=cols, lags=lags, scale=scale)
    return pl.pallas_call(
        kern,
        out_shape=jax.ShapeDtypeStruct((m, 1, lags), jnp.float32),
        compiler_params=pltpu.CompilerParams(vmem_limit_bytes=48 * 1024 * 1024),
    )(x, p)


def body(source_traces, receiver_traces, owners, source_alive, receiver_alive):
    lag_count = 2 * HALF + 1
    n_win = lax.axis_size("win")
    n_core = lax.axis_size("core")
    nt = source_traces.shape[2]
    rows = source_traces.shape[1] // n_win
    half = rows // n_core
    cols = -(-lag_count // 128) * 128
    per = -(-nt // half)
    extra = -(-per // 128) * 128
    scale = 1.0 / math.sqrt(n_win * nt)

    own_white = (
        flatten_rows(source_traces[0]) * source_alive.astype(jnp.float32)[:, None]
    ).astype(jnp.bfloat16)
    own_white = own_white[:, ::-1].reshape(n_win * n_core, half, nt)
    rcv_white = (
        spectral_flatten(receiver_traces[0]) * receiver_alive.astype(jnp.float32)[:, None]
    ).astype(jnp.bfloat16)
    rcv_rows = jnp.pad(rcv_white.reshape(-1), (0, half * per - nt)).reshape(half, per)
    rcv_rows = jnp.pad(rcv_rows, ((0, 0), (0, extra - per)))
    payload = jnp.concatenate(
        [own_white, jnp.broadcast_to(rcv_rows, (n_win * n_core, half, extra))], axis=2
    )
    got = lax.all_to_all(payload, ("win", "core"), 0, 0, tiled=True)
    got = got.reshape(n_win, n_core, half, nt + extra)

    my_core = lax.axis_index("core")
    my_chip = lax.axis_index("zz")
    n_chip = lax.axis_size("zz")
    src = got[..., :nt]
    chip_of = owners // n_core
    core_of = owners % n_core
    cores = jnp.arange(n_core, dtype=owners.dtype)
    chips = jnp.arange(n_chip, dtype=owners.dtype)
    wanted = jnp.any(
        (chip_of[:, None, None] == chips[None, :, None])
        & (core_of[:, None, None] == cores[None, None, :]),
        axis=0,
    )

    def ring_of(part):
        return jnp.stack([part] + [
            lax.ppermute(part, "zz", [(i, (i + j) % n_chip) for i in range(n_chip)])
            for j in range(1, n_chip)
        ])

    def steps_from(ring, pick_core):
        picked = []
        for k in range(STEPS):
            at = lax.rem(my_chip - chip_of[k] + n_chip, n_chip)
            block = lax.dynamic_index_in_dim(ring, at, 0, keepdims=False)
            if pick_core:
                block = lax.dynamic_index_in_dim(block, core_of[k], 1, keepdims=False)
            picked.append(block)
        return jnp.stack(picked, axis=1)

    def both_blocks(src):
        return steps_from(ring_of(src), True)

    def one_block(src):
        slot = jnp.argmax(wanted[my_chip]).astype(jnp.int32)
        part = lax.dynamic_index_in_dim(src, slot, 1, keepdims=False)
        return steps_from(ring_of(part), False)

    def one_double(c):
        def run(src):
            slot = jnp.argmax(wanted[my_chip]).astype(jnp.int32)
            part = lax.dynamic_index_in_dim(src, slot, 1, keepdims=False)
            first = steps_from(ring_of(part), False)
            extra = src[:, n_core - 1]
            second = jnp.where(my_chip == c, extra, jnp.zeros_like(extra))
            for j in range(1, n_chip):
                second = second + lax.ppermute(extra, "zz", [(c, (c + j) % n_chip)])
            late = owners == c * n_core + n_core - 1
            return jnp.where(late[None, :, None, None], second[:, None], first)
        return run

    doubles = jnp.sum(wanted.astype(jnp.int32), axis=1) == n_core
    n_doubles = jnp.sum(doubles.astype(jnp.int32))
    if n_chip <= 4 and n_core == 2:
        which = jnp.where(
            n_doubles == 0, 0,
            jnp.where(n_doubles == 1, 1 + jnp.argmax(doubles).astype(jnp.int32), n_chip + 1),
        )
        branches = [one_block] + [one_double(c) for c in range(n_chip)] + [both_blocks]
        mine_half = lax.switch(which, branches, src)
    else:
        mine_half = lax.cond(n_doubles == 0, one_block, both_blocks, src)
    other_half = lax.ppermute(mine_half, "core", [(0, 1), (1, 0)])
    blocks = jnp.where(
        my_core == 0,
        jnp.concatenate([mine_half, other_half], axis=2),
        jnp.concatenate([other_half, mine_half], axis=2),
    )
    x = blocks.reshape(n_win, STEPS * rows, nt)

    mine = lax.dynamic_index_in_dim(got, my_core, axis=1, keepdims=False)
    rcv_all = mine[:, :, nt:nt + per].reshape(n_win, half * per)[:, :nt]
    padded = jnp.pad(
        rcv_all, ((0, 0), (HALF + 1, cols - HALF - 1))
    )[:, None, :]

    out = correlate(x, padded, lag_count, scale)
    return out.reshape(STEPS, rows, 1, lag_count)


def solution(mesh):
    n_chan = mesh.shape["chan"]
    devices = mesh.devices.reshape(mesh.shape["win"], n_chan // 2, 2)
    sub = Mesh(devices, ("win", "zz", "core"))
    chan = ("zz", "core")
    placed = (P("win", chan, None), P("win", chan, None), P(), P(chan), P(chan))
    return jax.shard_map(
        body, mesh=sub, in_specs=placed, out_specs=P(None, "win", chan, None), check_vma=False
    )
```

```python
import functools
import math

import jax
import jax.numpy as jnp
from jax import lax
from jax.experimental import pallas as pl
from jax.experimental.pallas import tpu as pltpu
from jax.sharding import Mesh, PartitionSpec as P

HALF = 750
STEPS = 4
CHUNK = 256

epsilon_energy = 1e-06


def spectral_flatten(traces):
    row_entries, length = traces.shape
    values = traces.astype(jnp.float32).reshape(row_entries, length // 64, 64)
    power = jnp.mean(values * values, axis=-1, keepdims=True)
    return (values * lax.rsqrt(power + epsilon_energy)).reshape(row_entries, length)


def corr_kernel(x_ref, p_ref, o_ref, *, nt, cols, lags, scale):
    n_win, m, _ = x_ref.shape
    width = CHUNK + cols
    acc = jnp.zeros((m, cols), jnp.float32)
    for w in range(n_win):
        for i in range(nt // CHUNK):
            t0 = i * CHUNK
            start = nt - CHUNK - t0
            v = p_ref[w, :, start:start + width]
            rows = jnp.broadcast_to(v, (CHUNK, width))
            rolled = pltpu.roll(rows, 0, 1, stride=1, stride_axis=0)
            band = rolled[:, CHUNK:CHUNK + cols]
            acc = acc + jnp.dot(
                x_ref[w, :, t0:t0 + CHUNK], band, preferred_element_type=jnp.float32
            )
    o_ref[...] = (acc * scale)[:, :lags].reshape(m, 1, lags)


def correlate(x, p, lags, scale):
    n_win, m, nt = x.shape
    cols = p.shape[-1] - nt
    kern = functools.partial(corr_kernel, nt=nt, cols=cols, lags=lags, scale=scale)
    return pl.pallas_call(
        kern,
        out_shape=jax.ShapeDtypeStruct((m, 1, lags), jnp.float32),
        compiler_params=pltpu.CompilerParams(vmem_limit_bytes=48 * 1024 * 1024),
    )(x, p)


def body(source_traces, receiver_traces, owners, source_alive, receiver_alive):
    lag_count = 2 * HALF + 1
    n_win = lax.axis_size("win")
    n_core = lax.axis_size("core")
    nt = source_traces.shape[2]
    rows = source_traces.shape[1] // n_win
    half = rows // n_core
    cols = -(-lag_count // 128) * 128
    per = -(-nt // half)
    extra = -(-per // 128) * 128
    scale = 1.0 / math.sqrt(n_win * nt)

    own_white = (
        spectral_flatten(source_traces[0]) * source_alive.astype(jnp.float32)[:, None]
    ).astype(jnp.bfloat16)
    own_white = own_white[:, ::-1].reshape(n_win * n_core, half, nt)
    payload = own_white
    got = lax.all_to_all(payload, ("win", "core"), 0, 0, tiled=True)
    got = got.reshape(n_win, n_core, half, nt)

    my_core = lax.axis_index("core")
    my_chip = lax.axis_index("zz")
    n_chip = lax.axis_size("zz")
    src = got
    chip_of = owners // n_core
    core_of = owners % n_core
    cores = jnp.arange(n_core, dtype=owners.dtype)
    chips = jnp.arange(n_chip, dtype=owners.dtype)
    wanted = jnp.any(
        (chip_of[:, None, None] == chips[None, :, None])
        & (core_of[:, None, None] == cores[None, None, :]),
        axis=0,
    )

    def ring_of(part):
        return jnp.stack([part] + [
            lax.ppermute(part, "zz", [(i, (i + j) % n_chip) for i in range(n_chip)])
            for j in range(1, n_chip)
        ])

    def steps_from(ring, pick_core):
        picked = []
        for k in range(STEPS):
            at = lax.rem(my_chip - chip_of[k] + n_chip, n_chip)
            block = lax.dynamic_index_in_dim(ring, at, 0, keepdims=False)
            if pick_core:
                block = lax.dynamic_index_in_dim(block, core_of[k], 1, keepdims=False)
            picked.append(block)
        return jnp.stack(picked, axis=1)

    def both_blocks(src):
        return steps_from(ring_of(src), True)

    def one_block(src):
        slot = jnp.argmax(wanted[my_chip]).astype(jnp.int32)
        part = lax.dynamic_index_in_dim(src, slot, 1, keepdims=False)
        return steps_from(ring_of(part), False)

    def one_double(c):
        def run(src):
            slot = jnp.argmax(wanted[my_chip]).astype(jnp.int32)
            part = lax.dynamic_index_in_dim(src, slot, 1, keepdims=False)
            first = steps_from(ring_of(part), False)
            extra = src[:, n_core - 1]
            second = jnp.where(my_chip == c, extra, jnp.zeros_like(extra))
            for j in range(1, n_chip):
                second = second + lax.ppermute(extra, "zz", [(c, (c + j) % n_chip)])
            late = owners == c * n_core + n_core - 1
            return jnp.where(late[None, :, None, None], second[:, None], first)
        return run

    rcv_white = (
        spectral_flatten(receiver_traces[0]) * receiver_alive.astype(jnp.float32)[:, None]
    ).astype(jnp.bfloat16)
    my_win = lax.axis_index("win")
    shifted = jnp.concatenate([rcv_white] + [
        lax.ppermute(rcv_white, "win", [(i, (i + j) % n_win) for i in range(n_win)])
        for j in range(1, n_win)
    ])
    order = lax.rem(my_win - jnp.arange(n_win, dtype=jnp.int32) + n_win, n_win)
    rcv_all = jnp.take(shifted, order, axis=0)
    doubles = jnp.sum(wanted.astype(jnp.int32), axis=1) == n_core
    n_doubles = jnp.sum(doubles.astype(jnp.int32))
    if n_chip <= 4 and n_core == 2:
        which = jnp.where(
            n_doubles == 0, 0,
            jnp.where(n_doubles == 1, 1 + jnp.argmax(doubles).astype(jnp.int32), n_chip + 1),
        )
        branches = [one_block] + [one_double(c) for c in range(n_chip)] + [both_blocks]
    else:
        which = jnp.where(n_doubles == 0, 0, 1)
        branches = [one_block, both_blocks]
    src, rcv_all = lax.optimization_barrier((src, rcv_all))
    mine_half = lax.switch(which, branches, src)
    other_half = lax.ppermute(mine_half, "core", [(0, 1), (1, 0)])
    blocks = jnp.where(
        my_core == 0,
        jnp.concatenate([mine_half, other_half], axis=2),
        jnp.concatenate([other_half, mine_half], axis=2),
    )
    x = blocks.reshape(n_win, STEPS * rows, nt)

    padded = jnp.pad(
        rcv_all, ((0, 0), (HALF + 1, cols - HALF - 1))
    )[:, None, :]

    out = correlate(x, padded, lag_count, scale)
    return out.reshape(STEPS, rows, 1, lag_count)


def solution(mesh):
    n_chan = mesh.shape["chan"]
    devices = mesh.devices.reshape(mesh.shape["win"], n_chan // 2, 2)
    sub = Mesh(devices, ("win", "zz", "core"))
    chan = ("zz", "core")
    placed = (P("win", chan, None), P("win", chan, None), P(), P(chan), P(chan))
    return jax.shard_map(
        body, mesh=sub, in_specs=placed, out_specs=P(None, "win", chan, None), check_vma=False
    )
```

```python
import functools
import math

import jax
import jax.numpy as jnp
from jax import lax
from jax.experimental import pallas as pl
from jax.experimental.pallas import tpu as pltpu
from jax.sharding import Mesh, PartitionSpec as P

HALF = 750
STEPS = 4
CHUNK = 512

epsilon_energy = 1e-06


def spectral_flatten(traces):
    row_entries, length = traces.shape
    values = traces.astype(jnp.float32).reshape(row_entries, length // 64, 64)
    power = jnp.mean(values * values, axis=-1, keepdims=True)
    return (values * lax.rsqrt(power + epsilon_energy)).reshape(row_entries, length)


def corr_kernel(x_ref, p_ref, o_ref, *, nt, cols, lags, scale):
    n_win, m, _ = x_ref.shape
    width = CHUNK + cols
    acc = jnp.zeros((m, cols), jnp.float32)
    for w in range(n_win):
        for i in range(nt // CHUNK):
            t0 = i * CHUNK
            start = nt - CHUNK - t0
            v = p_ref[w, :, start:start + width]
            rows = jnp.broadcast_to(v, (CHUNK, width))
            rolled = pltpu.roll(rows, 0, 1, stride=1, stride_axis=0)
            band = rolled[:, CHUNK:CHUNK + cols]
            acc = acc + jnp.dot(
                x_ref[w, :, t0:t0 + CHUNK], band, preferred_element_type=jnp.float32
            )
    o_ref[...] = (acc * scale)[:, :lags].reshape(m, 1, lags)


def correlate(x, p, lags, scale):
    n_win, m, nt = x.shape
    cols = p.shape[-1] - nt
    kern = functools.partial(corr_kernel, nt=nt, cols=cols, lags=lags, scale=scale)
    return pl.pallas_call(
        kern,
        out_shape=jax.ShapeDtypeStruct((m, 1, lags), jnp.float32),
        compiler_params=pltpu.CompilerParams(vmem_limit_bytes=48 * 1024 * 1024),
    )(x, p)


def body(source_traces, receiver_traces, owners, source_alive, receiver_alive):
    lag_count = 2 * HALF + 1
    n_win = lax.axis_size("win")
    n_core = lax.axis_size("core")
    nt = source_traces.shape[2]
    rows = source_traces.shape[1] // n_win
    half = rows // n_core
    cols = -(-lag_count // 128) * 128
    per = -(-nt // half)
    extra = -(-per // 128) * 128
    scale = 1.0 / math.sqrt(n_win * nt)

    own_white = (
        spectral_flatten(source_traces[0]) * source_alive.astype(jnp.float32)[:, None]
    ).astype(jnp.bfloat16)
    own_white = own_white[:, ::-1].reshape(n_win * n_core, half, nt)
    rcv_white = (
        spectral_flatten(receiver_traces[0]) * receiver_alive.astype(jnp.float32)[:, None]
    ).astype(jnp.bfloat16)
    rcv_rows = jnp.pad(rcv_white.reshape(-1), (0, half * per - nt)).reshape(half, per)
    rcv_rows = jnp.pad(rcv_rows, ((0, 0), (0, extra - per)))
    payload = jnp.concatenate(
        [own_white, jnp.broadcast_to(rcv_rows, (n_win * n_core, half, extra))], axis=2
    )
    got = lax.all_to_all(payload, ("win", "core"), 0, 0, tiled=True)
    got = got.reshape(n_win, n_core, half, nt + extra)

    my_core = lax.axis_index("core")
    my_chip = lax.axis_index("zz")
    n_chip = lax.axis_size("zz")
    src = got[..., :nt]
    chip_of = owners // n_core
    core_of = owners % n_core
    cores = jnp.arange(n_core, dtype=owners.dtype)
    chips = jnp.arange(n_chip, dtype=owners.dtype)
    wanted = jnp.any(
        (chip_of[:, None, None] == chips[None, :, None])
        & (core_of[:, None, None] == cores[None, None, :]),
        axis=0,
    )

    def ring_of(part):
        return jnp.stack([part] + [
            lax.ppermute(part, "zz", [(i, (i + j) % n_chip) for i in range(n_chip)])
            for j in range(1, n_chip)
        ])

    def steps_from(ring, pick_core):
        picked = []
        for k in range(STEPS):
            at = lax.rem(my_chip - chip_of[k] + n_chip, n_chip)
            block = lax.dynamic_index_in_dim(ring, at, 0, keepdims=False)
            if pick_core:
                block = lax.dynamic_index_in_dim(block, core_of[k], 1, keepdims=False)
            picked.append(block)
        return jnp.stack(picked, axis=1)

    def both_blocks(src):
        return steps_from(ring_of(src), True)

    def one_block(src):
        slot = jnp.argmax(wanted[my_chip]).astype(jnp.int32)
        part = lax.dynamic_index_in_dim(src, slot, 1, keepdims=False)
        return steps_from(ring_of(part), False)

    def one_double(c):
        def run(src):
            slot = jnp.argmax(wanted[my_chip]).astype(jnp.int32)
            part = lax.dynamic_index_in_dim(src, slot, 1, keepdims=False)
            first = steps_from(ring_of(part), False)
            extra = src[:, n_core - 1]
            second = jnp.where(my_chip == c, extra, jnp.zeros_like(extra))
            for j in range(1, n_chip):
                second = second + lax.ppermute(extra, "zz", [(c, (c + j) % n_chip)])
            late = owners == c * n_core + n_core - 1
            return jnp.where(late[None, :, None, None], second[:, None], first)
        return run

    doubles = jnp.sum(wanted.astype(jnp.int32), axis=1) == n_core
    n_doubles = jnp.sum(doubles.astype(jnp.int32))
    if n_chip <= 4 and n_core == 2:
        which = jnp.where(
            n_doubles == 0, 0,
            jnp.where(n_doubles == 1, 1 + jnp.argmax(doubles).astype(jnp.int32), n_chip + 1),
        )
        branches = [one_block] + [one_double(c) for c in range(n_chip)] + [both_blocks]
        mine_half = lax.switch(which, branches, src)
    else:
        mine_half = lax.cond(n_doubles == 0, one_block, both_blocks, src)
    other_half = lax.ppermute(mine_half, "core", [(0, 1), (1, 0)])
    blocks = jnp.where(
        my_core == 0,
        jnp.concatenate([mine_half, other_half], axis=2),
        jnp.concatenate([other_half, mine_half], axis=2),
    )
    x = blocks.reshape(n_win, STEPS * rows, nt)

    mine = lax.dynamic_index_in_dim(got, my_core, axis=1, keepdims=False)
    rcv_all = mine[:, :, nt:nt + per].reshape(n_win, half * per)[:, :nt]
    padded = jnp.pad(
        rcv_all, ((0, 0), (HALF + 1, cols - HALF - 1))
    )[:, None, :]

    out = correlate(x, padded, lag_count, scale)
    return out.reshape(STEPS, rows, 1, lag_count)


def solution(mesh):
    n_chan = mesh.shape["chan"]
    devices = mesh.devices.reshape(mesh.shape["win"], n_chan // 2, 2)
    sub = Mesh(devices, ("win", "zz", "core"))
    chan = ("zz", "core")
    placed = (P("win", chan, None), P("win", chan, None), P(), P(chan), P(chan))
    return jax.shard_map(
        body, mesh=sub, in_specs=placed, out_specs=P(None, "win", chan, None), check_vma=False
    )
```

```python
import functools
import math

import jax
import jax.numpy as jnp
from jax import lax
from jax.experimental import pallas as pl
from jax.experimental.pallas import tpu as pltpu
from jax.sharding import Mesh, PartitionSpec as P

HALF = 750
STEPS = 4
CHUNK = 512

epsilon_energy = 1e-06


def spectral_flatten(traces):
    row_entries, length = traces.shape
    values = traces.astype(jnp.float32).reshape(row_entries, length // 64, 64)
    power = jnp.mean(values * values, axis=-1, keepdims=True)
    return (values * lax.rsqrt(power + epsilon_energy)).reshape(row_entries, length)


def corr_kernel(c_ref, xm_ref, xo_ref, p_ref, o_ref, *, nt, cols, lags, scale):
    n_win, n_k, h, _ = xm_ref.shape
    width = CHUNK + cols
    acc = jnp.zeros((n_k * 2 * h, cols), jnp.float32)
    for w in range(n_win):
        for i in range(nt // CHUNK):
            t0 = i * CHUNK
            start = nt - CHUNK - t0
            v = p_ref[w, :, start:start + width]
            rows = jnp.broadcast_to(v, (CHUNK, width))
            rolled = pltpu.roll(rows, 0, 1, stride=1, stride_axis=0)
            band = rolled[:, CHUNK:CHUNK + cols]
            lhs = jnp.concatenate(
                [r[w, k, :, t0:t0 + CHUNK] for k in range(n_k) for r in (xm_ref, xo_ref)],
                axis=0,
            )
            acc = acc + jnp.dot(lhs, band, preferred_element_type=jnp.float32)
    res = (acc * scale)[:, :lags].reshape(n_k * 2 * h, 1, lags)
    core = c_ref[0]
    for k in range(n_k):
        base = k * 2 * h
        o_ref[pl.ds(base + core * h, h)] = res[base:base + h]
        o_ref[pl.ds(base + (1 - core) * h, h)] = res[base + h:base + 2 * h]


def correlate(core, xm, xo, p, lags, scale):
    n_win, n_k, h, nt = xm.shape
    cols = p.shape[-1] - nt
    kern = functools.partial(corr_kernel, nt=nt, cols=cols, lags=lags, scale=scale)
    vmem = pl.BlockSpec(memory_space=pltpu.VMEM)
    return pl.pallas_call(
        kern,
        out_shape=jax.ShapeDtypeStruct((n_k * 2 * h, 1, lags), jnp.float32),
        in_specs=[pl.BlockSpec(memory_space=pltpu.SMEM), vmem, vmem, vmem],
        out_specs=vmem,
        compiler_params=pltpu.CompilerParams(vmem_limit_bytes=48 * 1024 * 1024),
    )(core, xm, xo, p)


def body(source_traces, receiver_traces, owners, source_alive, receiver_alive):
    lag_count = 2 * HALF + 1
    n_win = lax.axis_size("win")
    n_core = lax.axis_size("core")
    nt = source_traces.shape[2]
    rows = source_traces.shape[1] // n_win
    half = rows // n_core
    cols = -(-lag_count // 128) * 128
    per = -(-nt // half)
    extra = -(-per // 128) * 128
    scale = 1.0 / math.sqrt(n_win * nt)

    own_white = (
        spectral_flatten(source_traces[0]) * source_alive.astype(jnp.float32)[:, None]
    ).astype(jnp.bfloat16)
    own_white = own_white[:, ::-1].reshape(n_win * n_core, half, nt)
    rcv_white = (
        spectral_flatten(receiver_traces[0]) * receiver_alive.astype(jnp.float32)[:, None]
    ).astype(jnp.bfloat16)
    rcv_rows = jnp.pad(rcv_white.reshape(-1), (0, half * per - nt)).reshape(half, per)
    rcv_rows = jnp.pad(rcv_rows, ((0, 0), (0, extra - per)))
    payload = jnp.concatenate(
        [own_white, jnp.broadcast_to(rcv_rows, (n_win * n_core, half, extra))], axis=2
    )
    got = lax.all_to_all(payload, ("win", "core"), 0, 0, tiled=True)
    got = got.reshape(n_win, n_core, half, nt + extra)

    my_core = lax.axis_index("core")
    my_chip = lax.axis_index("zz")
    n_chip = lax.axis_size("zz")
    src = got[..., :nt]
    chip_of = owners // n_core
    core_of = owners % n_core
    cores = jnp.arange(n_core, dtype=owners.dtype)
    chips = jnp.arange(n_chip, dtype=owners.dtype)
    wanted = jnp.any(
        (chip_of[:, None, None] == chips[None, :, None])
        & (core_of[:, None, None] == cores[None, None, :]),
        axis=0,
    )

    def ring_of(part):
        return jnp.stack([part] + [
            lax.ppermute(part, "zz", [(i, (i + j) % n_chip) for i in range(n_chip)])
            for j in range(1, n_chip)
        ])

    def steps_from(ring, pick_core):
        picked = []
        for k in range(STEPS):
            at = lax.rem(my_chip - chip_of[k] + n_chip, n_chip)
            block = lax.dynamic_index_in_dim(ring, at, 0, keepdims=False)
            if pick_core:
                block = lax.dynamic_index_in_dim(block, core_of[k], 1, keepdims=False)
            picked.append(block)
        return jnp.stack(picked, axis=1)

    def both_blocks(src):
        return steps_from(ring_of(src), True)

    def one_block(src):
        slot = jnp.argmax(wanted[my_chip]).astype(jnp.int32)
        part = lax.dynamic_index_in_dim(src, slot, 1, keepdims=False)
        return steps_from(ring_of(part), False)

    def one_double(c):
        def run(src):
            slot = jnp.argmax(wanted[my_chip]).astype(jnp.int32)
            part = lax.dynamic_index_in_dim(src, slot, 1, keepdims=False)
            first = steps_from(ring_of(part), False)
            extra = src[:, n_core - 1]
            second = jnp.where(my_chip == c, extra, jnp.zeros_like(extra))
            for j in range(1, n_chip):
                second = second + lax.ppermute(extra, "zz", [(c, (c + j) % n_chip)])
            late = owners == c * n_core + n_core - 1
            return jnp.where(late[None, :, None, None], second[:, None], first)
        return run

    doubles = jnp.sum(wanted.astype(jnp.int32), axis=1) == n_core
    n_doubles = jnp.sum(doubles.astype(jnp.int32))
    if n_chip <= 4 and n_core == 2:
        which = jnp.where(
            n_doubles == 0, 0,
            jnp.where(n_doubles == 1, 1 + jnp.argmax(doubles).astype(jnp.int32), n_chip + 1),
        )
        branches = [one_block] + [one_double(c) for c in range(n_chip)] + [both_blocks]
        mine_half = lax.switch(which, branches, src)
    else:
        mine_half = lax.cond(n_doubles == 0, one_block, both_blocks, src)
    other_half = lax.ppermute(mine_half, "core", [(0, 1), (1, 0)])

    mine = lax.dynamic_index_in_dim(got, my_core, axis=1, keepdims=False)
    rcv_all = mine[:, :, nt:nt + per].reshape(n_win, half * per)[:, :nt]
    padded = jnp.pad(
        rcv_all, ((0, 0), (HALF + 1, cols - HALF - 1))
    )[:, None, :]

    core_id = my_core.astype(jnp.int32).reshape(1)
    out = correlate(core_id, mine_half, other_half, padded, lag_count, scale)
    return out.reshape(STEPS, rows, 1, lag_count)


def solution(mesh):
    n_chan = mesh.shape["chan"]
    devices = mesh.devices.reshape(mesh.shape["win"], n_chan // 2, 2)
    sub = Mesh(devices, ("win", "zz", "core"))
    chan = ("zz", "core")
    placed = (P("win", chan, None), P("win", chan, None), P(), P(chan), P(chan))
    return jax.shard_map(
        body, mesh=sub, in_specs=placed, out_specs=P(None, "win", chan, None), check_vma=False
    )
```
